256 devices in a mesh: segment: 4 (over z_lo), expert: 64 (over x, y, z_hi, core).
Axes of the slice: x: 4, y: 4, z: 8 (z_hi: 2, z_lo: 4; z = z_hi * 4 + z_lo), core: 2. Of those that a mesh axis runs over, the one named last changes fastest.
Arguments:
- forward_input: bfloat16 [4, 512, 7168], P('segment', 'expert'), may hold values from -6 to 6
- forward_routes: int32 [4, 512, 8], P('segment', 'expert'), may hold values from 0 to 15, all different within a row; in each aligned block of 8 rows (0 to 7, 8 to 15, ..., all dimensions but the last counted through in order) at most 8 rows name the same one
- forward_gates: float32 [4, 512, 8], P('segment', 'expert'), may hold values from 0.05 to 0.8
- gate_matrix: bfloat16 [4, 64, 7168, 256], P('segment', 'expert'), may hold values from -0.0625 to 0.0625
- up_matrix: bfloat16 [4, 64, 7168, 256], P('segment', 'expert'), may hold values from -0.0625 to 0.0625
- down_matrix: bfloat16 [4, 64, 256, 7168], P('segment', 'expert'), may hold values from -0.1875 to 0.1875
Outputs:
- next_input: bfloat16 [4, 512, 7168], P('segment', 'expert')
The draws below stay inside these ranges and needn't reach their ends.
Inputs may be any that keep to these rules, and one draw needn't show every extreme that they name: `forward_routes`: each token names 8 different experts. Among the 8 tokens of one index of expert, no expert is named by more than 8 of them, and in every draw some expert is named by exactly 8 tokens of some index.
All inputs are finite; a program needn't handle non-finite values.
Results may differ from the reference program's by a relative error of at most 0.0065.
Values may be sent and summed in bfloat16 or wider, within the bound.
No kernel may reach another device: no remote copies, remote signals or barrier semaphores. Data moves between devices by JAX's collectives and lax.ppermute only.
A program may use at most 128 MiB of HBM per device.

```python
import math
import jax
import jax.numpy as jnp
import numpy as np
from jax import lax

D = 7168
TOPK = 8
FH = 1024
TOK = 8
SPLIT = 4
EXPERTS = 16
FH_DEV = 256
TOKENS = 512
CAP = 8
N_SEGMENT = 4
N_EXPERT = 64


def level_of(rng, shape, cuts, smallest, high):
    factor_of = 1.0
    for dim, shards_of in cuts:
        heights = jax.random.uniform(jax.random.fold_in(jax.random.fold_in(rng, 6), dim), (shards_of,), jnp.float32, smallest / len(cuts), high / len(cuts))
        factor_of = factor_of * jnp.repeat(jnp.exp(heights), shape[dim] // shards_of).reshape((-1,) + (1,) * (len(shape) - 1 - dim))
    return factor_of


def assign_block(rng, own, number, rows, number_of, top, limit, slope):
    order = jax.random.permutation(rng, number_of)
    crowded, ordinary = load_shares(number_of, rows * top, limit, slope, True), load_shares(number_of, rows * top, limit, slope, False)
    places = jnp.arange(number_of)

    def named(tallies, turn):
        used = int((tallies > 0).sum())
        fixed = max(1, used // 4)
        shifted = fixed + (places - fixed + turn * (used - fixed)) % max(1, number_of - fixed)
        return jnp.zeros((number_of,), jnp.int32).at[order[jnp.where(places < fixed, places, shifted)]].set(jnp.asarray(tallies, jnp.int32))

    tallies = jnp.where(number % 4 == 0, named(crowded, number // 4), named(ordinary, number - number // 4 - 1))
    mixed = jax.random.permutation(jax.random.fold_in(own, 3), number_of)
    source_of, sink = mixed[0:number_of // 2 * 2:2], mixed[1:number_of // 2 * 2:2]
    room = jnp.minimum(tallies[source_of] - 1, limit - tallies[sink]) // 2
    room = jnp.where((source_of == order[0]) | (sink == order[0]) | (tallies[sink] == 0), 0, jnp.maximum(room, 0))
    shifted = jax.random.randint(jax.random.fold_in(own, 4), (number_of // 2,), 0, 1 << 20) % (room + 1)
    tallies = tallies.at[source_of].add(-shifted).at[sink].add(shifted)
    members = jnp.searchsorted(jnp.cumsum(tallies), jnp.arange(rows * top), side="right").astype(jnp.int32)
    listing = members.reshape(top, rows).T
    listing = listing[jax.random.permutation(jax.random.fold_in(own, 1), rows)]
    turn = jax.random.randint(jax.random.fold_in(own, 2), (rows, 1), 0, top)
    return jnp.take_along_axis(listing, (jnp.arange(top)[None, :] + turn) % top, axis=1)


def load_shares(count, total, bound, slope, full):
    portions = [(1 << 20) // math.isqrt(rank ** slope) + 1 for rank in range(1, count + 1)]
    largest = bound if full else min(bound, max(-(-total // count), total * portions[0] // sum(portions)))
    least = 1 if total - largest >= count - 1 else 0
    counts, rest = [largest] + [least] * (count - 1), total - largest - least * (count - 1)
    while rest > 0:
        movable = [i for i in range(1, count) if counts[i] < largest] or [i for i in range(1, count) if counts[i] < bound]
        pool, budget = sum([portions[i] for i in movable]), rest
        for i in movable:
            addition = min(bound - counts[i], max(1, budget * portions[i] // pool), rest)
            counts[i] = counts[i] + addition
            rest = rest - addition
    return np.array(counts)


def noise(own_key, extent, spread, most, shards=(), held_as=jnp.bfloat16):
    values = spread * jax.random.normal(own_key, extent, jnp.float32)
    if shards:
        values = values * level_of(own_key, extent, shards, -0.22, 0.18)
    return jnp.clip(values, -most, most).astype(held_as)


def setup_inputs(seed: int = 0) -> dict:
    keys = jax.random.split(jax.random.key(seed), 7)
    forward_input = noise(keys[0], (N_SEGMENT, TOKENS, D), 1.0, 6.0, ((0, 4), (1, 64)))
    forward_routes_keys = jax.random.split(jax.random.fold_in(keys[1], 1), N_SEGMENT * TOKENS // TOK)
    forward_routes_turns = jax.random.permutation(jax.random.fold_in(keys[1], 3), N_SEGMENT * TOKENS // TOK)
    forward_routes = jax.vmap(lambda own, number: assign_block(jax.random.fold_in(keys[1], 2), own, number, TOK, EXPERTS, TOPK, CAP, 2))(forward_routes_keys, forward_routes_turns).reshape((N_SEGMENT, TOKENS, TOPK))
    forward_gates = jnp.clip(jnp.exp(math.log(0.8) - 2.7725887 * jax.random.uniform(keys[2], (N_SEGMENT, TOKENS, TOPK), jnp.float32) ** level_of(keys[2], (N_SEGMENT, TOKENS, TOPK), ((0, 4), (1, 64)), -0.2, 0.2)), 0.05, 0.8)
    gate_matrix = noise(keys[3], (N_SEGMENT, N_EXPERT, D, FH_DEV), D ** -0.5, 0.0625, ((0, 4), (1, 64)))
    up_matrix = noise(keys[4], (N_SEGMENT, N_EXPERT, D, FH_DEV), D ** -0.5, 0.0625, ((0, 4), (1, 64)))
    down_matrix = noise(keys[5], (N_SEGMENT, N_EXPERT, FH_DEV, D), FH ** -0.5, 0.1875, ((0, 4), (1, 64)))
    return dict(forward_input=forward_input, forward_routes=forward_routes, forward_gates=forward_gates, gate_matrix=gate_matrix, up_matrix=up_matrix, down_matrix=down_matrix)


def slot_table(routes, experts, capacity):
    route_count = routes.shape[0] * routes.shape[1]
    flat_routes = routes.reshape(-1)
    onehot = (flat_routes[:, None] == jnp.arange(experts, dtype=jnp.int32)[None, :]).astype(jnp.int32)
    before = jnp.cumsum(onehot, axis=0) - onehot
    ranking = jnp.sum(before * onehot, axis=1).astype(jnp.int32)
    position = (flat_routes * capacity + ranking).astype(jnp.int32)
    source_row = jnp.zeros((experts * capacity,), jnp.int32).at[position].set(jnp.arange(route_count, dtype=jnp.int32))
    filled = jnp.zeros((experts * capacity,), jnp.int32).at[position].set(1)
    return position, source_row, filled


def expert_forward(row_block, gate_mat, upper_mat, down_mat):
    gate_act = jnp.dot(row_block, gate_mat, preferred_element_type=jnp.float32)
    upper_act = jnp.dot(row_block, upper_mat, preferred_element_type=jnp.float32)
    hidden = (jax.nn.silu(gate_act) * upper_act).astype(jnp.bfloat16)
    return jnp.dot(hidden, down_mat, preferred_element_type=jnp.float32).astype(jnp.bfloat16)


def section_forward(tokens, routes, gates, gate_mat, upper_mat, down_mat):
    sources = N_EXPERT
    groups = EXPERTS
    capacity = CAP
    blocks = tokens.reshape(sources, TOK, D)
    route_blocks = routes.reshape(sources, TOK, TOPK)
    gate_blocks = gates.reshape(sources, TOK, TOPK)
    position, source_row, filled = jax.vmap(lambda single: slot_table(single, groups, capacity))(route_blocks)

    def pack(token_block, source, filled_mask):
        return jnp.where(filled_mask[:, None] > 0, token_block[source // TOPK], jnp.zeros((), tokens.dtype))

    sent = jax.vmap(pack)(blocks, source_row, filled).reshape(sources, groups, capacity, D)
    received = jnp.transpose(sent, (1, 0, 2, 3))
    gate_split = jnp.transpose(gate_mat.reshape(SPLIT, groups, D, FH_DEV), (1, 0, 2, 3))
    upper_split = jnp.transpose(upper_mat.reshape(SPLIT, groups, D, FH_DEV), (1, 0, 2, 3))
    down_split = jnp.transpose(down_mat.reshape(SPLIT, groups, FH_DEV, D), (1, 0, 2, 3))

    def per_expert(packed):
        rows, gate_part, upper_part, down_part = packed
        flat = rows.reshape(-1, D)

        def per_slice(total, pieces):
            return total + expert_forward(flat, pieces[0], pieces[1], pieces[2]).astype(jnp.float32), None

        total, _ = lax.scan(per_slice, jnp.zeros((flat.shape[0], D), jnp.float32), (gate_part, upper_part, down_part))
        return total.astype(jnp.bfloat16).reshape(sources, capacity, D)

    results = lax.map(per_expert, (received, gate_split, upper_split, down_split))
    returned = jnp.transpose(results, (1, 0, 2, 3)).reshape(sources, groups * capacity, D)

    def combine(back_rows, places, weights, token_block):
        picked = back_rows[places].astype(jnp.float32).reshape(TOK, TOPK, D)
        mixed = jnp.einsum("tk,tkd->td", weights.astype(jnp.float32), picked)
        return (token_block.astype(jnp.float32) + mixed).astype(jnp.bfloat16)

    return jax.vmap(combine)(returned, position, gate_blocks, blocks).reshape(TOKENS, D)


def reference(forward_input, forward_routes, forward_gates, gate_matrix, up_matrix, down_matrix):
    layer_list = []
    for section in range(N_SEGMENT):
        layer_list.append(section_forward(forward_input[section], forward_routes[section], forward_gates[section], gate_matrix[section], up_matrix[section], down_matrix[section]))
    layer_out = jnp.stack(layer_list)
    return jnp.roll(layer_out, 1, axis=0)
```

```python
import jax
import jax.numpy as jnp
from jax import lax
from jax.sharding import PartitionSpec as P

FH = 1024


def passed_along(value, axis, steps):
    count = lax.axis_size(axis)
    pairs = [(source, (source + steps) % count) for source in range(count)]
    return lax.ppermute(value, axis, pairs)


def local(forward_input, forward_routes, forward_gates, gate_matrix, up_matrix, down_matrix):
    devices = lax.axis_size("expert")
    hidden_slice = gate_matrix.shape[3]
    split = FH // hidden_slice
    groups = devices // split
    tokens = forward_input[0]
    me = lax.axis_index("expert")
    expert = me % groups
    rows = lax.all_gather(tokens, "expert", axis=0, tiled=True)
    routes = lax.all_gather(forward_routes[0], "expert", axis=0, tiled=True)
    gates = lax.all_gather(forward_gates[0], "expert", axis=0, tiled=True)
    weight = jnp.sum(jnp.where(routes == expert, gates, 0.0), axis=1)
    gate_act = jnp.dot(rows, gate_matrix[0, 0], preferred_element_type=jnp.float32)
    upper_act = jnp.dot(rows, up_matrix[0, 0], preferred_element_type=jnp.float32)
    hidden = (jax.nn.silu(gate_act) * upper_act).astype(jnp.bfloat16)
    partial = jnp.dot(hidden, down_matrix[0, 0], preferred_element_type=jnp.float32)
    partial = partial.astype(jnp.bfloat16).astype(jnp.float32)
    weighted = (weight[:, None] * partial).astype(jnp.bfloat16)
    mixed = lax.psum_scatter(weighted, "expert", scatter_dimension=0, tiled=True)
    layer_out = (tokens.astype(jnp.float32) + mixed.astype(jnp.float32)).astype(jnp.bfloat16)
    next_input = passed_along(layer_out, "segment", 1)
    return next_input[None]


def solution(mesh):
    in_specs = (
        P("segment", "expert", None),
        P("segment", "expert", None),
        P("segment", "expert", None),
        P("segment", "expert", None, None),
        P("segment", "expert", None, None),
        P("segment", "expert", None, None),
    )
    out_specs = P("segment", "expert", None)
    return jax.shard_map(local, mesh=mesh, in_specs=in_specs, out_specs=out_specs, check_vma=False)
```

```python
import jax
import jax.numpy as jnp
from jax import lax
from jax.sharding import PartitionSpec as P

FH = 1024
X_SIZE, Y_SIZE, Z_SIZE, C_SIZE = 4, 4, 2, 2


def coords(e):
    return (e // (Y_SIZE * Z_SIZE * C_SIZE), (e // (Z_SIZE * C_SIZE)) % Y_SIZE, (e // C_SIZE) % Z_SIZE, e % C_SIZE)


def index_of(x, y, z, c):
    return ((x * Y_SIZE + y) * Z_SIZE + z) * C_SIZE + c


def moved(value, target):
    count = X_SIZE * Y_SIZE * Z_SIZE * C_SIZE
    pairs = [(e, target(*coords(e))) for e in range(count)]
    return lax.ppermute(value, "expert", pairs)


def passed_along(value, axis, steps):
    count = lax.axis_size(axis)
    pairs = [(source, (source + steps) % count) for source in range(count)]
    return lax.ppermute(value, axis, pairs)


PLANE = [(dx, dy) for dx in range(X_SIZE) for dy in range(Y_SIZE) if (dx, dy) != (0, 0)]


def ahead(dx, dy):
    return lambda x, y, z, c: index_of((x + dx) % X_SIZE, (y + dy) % Y_SIZE, z, c)


def behind(dx, dy):
    return lambda x, y, z, c: index_of((x - dx) % X_SIZE, (y - dy) % Y_SIZE, z, c)


def across_z(x, y, z, c):
    return index_of(x, y, 1 - z, c)


def across_core(x, y, z, c):
    return index_of(x, y, z, 1 - c)


def expert_rows(rows, weight, gate_mat, upper_mat, down_mat):
    gate_act = jnp.dot(rows, gate_mat, preferred_element_type=jnp.float32)
    upper_act = jnp.dot(rows, upper_mat, preferred_element_type=jnp.float32)
    hidden = (jax.nn.silu(gate_act) * upper_act).astype(jnp.bfloat16)
    part = jnp.dot(hidden, down_mat, preferred_element_type=jnp.float32)
    return weight[:, None] * part.astype(jnp.bfloat16).astype(jnp.float32)


def local(forward_input, forward_routes, forward_gates, gate_matrix, up_matrix, down_matrix):
    devices = lax.axis_size("expert")
    hidden_slice = gate_matrix.shape[3]
    split = FH // hidden_slice
    groups = devices // split
    tokens = forward_input[0]
    width = tokens.shape[1]
    me = lax.axis_index("expert")
    expert = me % groups
    named = forward_routes[0][:, :, None] == jnp.arange(groups, dtype=jnp.int32)[None, None, :]
    coef = jnp.sum(jnp.where(named, forward_gates[0][:, :, None], 0.0), axis=1)

    col = (tokens, coef)
    zx = moved(col, across_z)
    col = tuple(jnp.stack([a, b]) for a, b in zip(col, zx))
    plane = [col] + [moved(col, ahead(dx, dy)) for dx, dy in PLANE]
    plane = tuple(jnp.stack([p[i] for p in plane]) for i in range(2))
    other = moved(plane, across_core)

    mats = (gate_matrix[0, 0], up_matrix[0, 0], down_matrix[0, 0])
    pick = (jnp.arange(groups) == expert).astype(jnp.float32)
    own_rows = plane[0].reshape(-1, width)
    own_w = jnp.sum(plane[1].reshape(-1, groups) * pick, axis=1)
    other_rows = other[0].reshape(-1, width)
    other_w = jnp.sum(other[1].reshape(-1, groups) * pick, axis=1)
    other_part = expert_rows(other_rows, other_w, *mats)
    back = moved(other_part.astype(jnp.bfloat16), across_core)
    own_part = expert_rows(own_rows, own_w, *mats)
    summed = own_part + back.astype(jnp.float32)
    summed = summed.reshape((len(PLANE) + 1, 2) + tokens.shape)

    total = summed[0]
    sent = summed.astype(jnp.bfloat16)
    for s, (dx, dy) in enumerate(PLANE):
        total = total + moved(sent[s + 1], behind(dx, dy)).astype(jnp.float32)
    mine = total[0] + moved(total[1].astype(jnp.bfloat16), across_z).astype(jnp.float32)
    layer_out = (tokens.astype(jnp.float32) + mine).astype(jnp.bfloat16)
    next_input = passed_along(layer_out, "segment", 1)
    return next_input[None]


def solution(mesh):
    in_specs = (
        P("segment", "expert", None),
        P("segment", "expert", None),
        P("segment", "expert", None),
        P("segment", "expert", None, None),
        P("segment", "expert", None, None),
        P("segment", "expert", None, None),
    )
    out_specs = P("segment", "expert", None)
    return jax.shard_map(local, mesh=mesh, in_specs=in_specs, out_specs=out_specs, check_vma=False)
```

```python
import jax
import jax.numpy as jnp
from jax import lax
from jax.sharding import PartitionSpec as P

FH = 1024
X_SIZE, Y_SIZE, Z_SIZE, C_SIZE = 4, 4, 2, 2


def coords(e):
    return (e // (Y_SIZE * Z_SIZE * C_SIZE), (e // (Z_SIZE * C_SIZE)) % Y_SIZE, (e // C_SIZE) % Z_SIZE, e % C_SIZE)


def index_of(x, y, z, c):
    return ((x * Y_SIZE + y) * Z_SIZE + z) * C_SIZE + c


def moved(value, target):
    count = X_SIZE * Y_SIZE * Z_SIZE * C_SIZE
    pairs = [(e, target(*coords(e))) for e in range(count)]
    return lax.ppermute(value, "expert", pairs)


def passed_along(value, axis, steps):
    count = lax.axis_size(axis)
    pairs = [(source, (source + steps) % count) for source in range(count)]
    return lax.ppermute(value, axis, pairs)


def along(axis, step):
    def target(x, y, z, c):
        first = axis if c == 0 else 1 - axis
        if first == 0:
            return index_of((x + step) % X_SIZE, y, z, c)
        return index_of(x, (y + step) % Y_SIZE, z, c)

    return target


def across_z(x, y, z, c):
    return index_of(x, y, 1 - z, c)


def across_core(x, y, z, c):
    return index_of(x, y, z, 1 - c)


def expert_rows(rows, weight, gate_mat, upper_mat, down_mat):
    gate_act = jnp.dot(rows, gate_mat, preferred_element_type=jnp.float32)
    upper_act = jnp.dot(rows, upper_mat, preferred_element_type=jnp.float32)
    hidden = (jax.nn.silu(gate_act) * upper_act).astype(jnp.bfloat16)
    part = jnp.dot(hidden, down_mat, preferred_element_type=jnp.float32)
    return weight[:, None] * part.astype(jnp.bfloat16).astype(jnp.float32)


def coded(coef):
    first = coef.astype(jnp.bfloat16)
    rest = coef - first.astype(jnp.float32)
    second = rest.astype(jnp.bfloat16)
    third = (rest - second.astype(jnp.float32)).astype(jnp.bfloat16)
    return jnp.concatenate([first, second, third], axis=-1)


def decoded(code, groups):
    code = code.astype(jnp.float32)
    return code[..., :groups] + code[..., groups:2 * groups] + code[..., 2 * groups:3 * groups]


def local(forward_input, forward_routes, forward_gates, gate_matrix, up_matrix, down_matrix):
    devices = lax.axis_size("expert")
    hidden_slice = gate_matrix.shape[3]
    split = FH // hidden_slice
    groups = devices // split
    tokens = forward_input[0]
    width = tokens.shape[1]
    me = lax.axis_index("expert")
    expert = me % groups
    named = forward_routes[0][:, :, None] == jnp.arange(groups, dtype=jnp.int32)[None, None, :]
    coef = jnp.sum(jnp.where(named, forward_gates[0][:, :, None], 0.0), axis=1)
    code = coded(coef)
    pad = 128 * ((code.shape[1] + 127) // 128) - code.shape[1]
    code = jnp.pad(code, ((0, 0), (0, pad)))
    col = jnp.concatenate([tokens, code], axis=1)

    col = jnp.stack([col, moved(col, across_z)])
    ring = X_SIZE
    first = jnp.stack([col] + [moved(col, along(0, k)) for k in range(1, ring)])
    second = jnp.stack([first] + [moved(first, along(1, k)) for k in range(1, ring)])
    other = moved(second, across_core)

    mats = (gate_matrix[0, 0], up_matrix[0, 0], down_matrix[0, 0])
    own_rows = second[..., :width].reshape(-1, width)
    own_w = decoded(second[..., width:].reshape(own_rows.shape[0], -1), groups)[:, expert]
    other_rows = other[..., :width].reshape(-1, width)
    other_w = decoded(other[..., width:].reshape(other_rows.shape[0], -1), groups)[:, expert]
    other_part = expert_rows(other_rows, other_w, *mats)
    back = moved(other_part.astype(jnp.bfloat16), across_core)
    own_part = expert_rows(own_rows, own_w, *mats)
    summed = own_part + back.astype(jnp.float32)
    summed = summed.reshape((ring, ring, 2) + tokens.shape)

    total = summed[0]
    sent = summed.astype(jnp.bfloat16)
    for m in range(1, ring):
        total = total + moved(sent[m], along(1, -m)).astype(jnp.float32)
    total_first = total[0]
    sent = total.astype(jnp.bfloat16)
    for k in range(1, ring):
        total_first = total_first + moved(sent[k], along(0, -k)).astype(jnp.float32)
    mine = total_first[0] + moved(total_first[1].astype(jnp.bfloat16), across_z).astype(jnp.float32)
    layer_out = (tokens.astype(jnp.float32) + mine).astype(jnp.bfloat16)
    next_input = passed_along(layer_out, "segment", 1)
    return next_input[None]


def solution(mesh):
    in_specs = (
        P("segment", "expert", None),
        P("segment", "expert", None),
        P("segment", "expert", None),
        P("segment", "expert", None, None),
        P("segment", "expert", None, None),
        P("segment", "expert", None, None),
    )
    out_specs = P("segment", "expert", None)
    return jax.shard_map(local, mesh=mesh, in_specs=in_specs, out_specs=out_specs, check_vma=False)
```

```python
import jax
import jax.numpy as jnp
from jax import lax
from jax.sharding import PartitionSpec as P

FH = 1024
X_SIZE, Y_SIZE, Z_SIZE, C_SIZE = 4, 4, 2, 2


def coords(e):
    return (e // (Y_SIZE * Z_SIZE * C_SIZE), (e // (Z_SIZE * C_SIZE)) % Y_SIZE, (e // C_SIZE) % Z_SIZE, e % C_SIZE)


def index_of(x, y, z, c):
    return ((x * Y_SIZE + y) * Z_SIZE + z) * C_SIZE + c


def moved(value, target):
    count = X_SIZE * Y_SIZE * Z_SIZE * C_SIZE
    pairs = [(e, target(*coords(e))) for e in range(count)]
    return lax.ppermute(value, "expert", pairs)


def passed_along(value, axis, steps):
    count = lax.axis_size(axis)
    pairs = [(source, (source + steps) % count) for source in range(count)]
    return lax.ppermute(value, axis, pairs)


def along(axis, step):
    def target(x, y, z, c):
        first = axis if c == 0 else 1 - axis
        if first == 0:
            return index_of((x + step) % X_SIZE, y, z, c)
        return index_of(x, (y + step) % Y_SIZE, z, c)

    return target


def across_z(x, y, z, c):
    return index_of(x, y, 1 - z, c)


def across_core(x, y, z, c):
    return index_of(x, y, z, 1 - c)


def expert_rows(rows, weight, gate_mat, upper_mat, down_mat):
    gate_act = jnp.dot(rows, gate_mat, preferred_element_type=jnp.float32)
    upper_act = jnp.dot(rows, upper_mat, preferred_element_type=jnp.float32)
    hidden = (jax.nn.silu(gate_act) * upper_act).astype(jnp.bfloat16)
    part = jnp.dot(hidden, down_mat, preferred_element_type=jnp.float32)
    return weight[:, None] * part.astype(jnp.bfloat16).astype(jnp.float32)


def coded(coef):
    first = coef.astype(jnp.bfloat16)
    rest = coef - first.astype(jnp.float32)
    second = rest.astype(jnp.bfloat16)
    third = (rest - second.astype(jnp.float32)).astype(jnp.bfloat16)
    return jnp.concatenate([first, second, third], axis=-1)


def decoded(code, groups):
    code = code.astype(jnp.float32)
    return code[..., :groups] + code[..., groups:2 * groups] + code[..., 2 * groups:3 * groups]


def local(forward_input, forward_routes, forward_gates, gate_matrix, up_matrix, down_matrix):
    devices = lax.axis_size("expert")
    hidden_slice = gate_matrix.shape[3]
    split = FH // hidden_slice
    groups = devices // split
    tokens = forward_input[0]
    width = tokens.shape[1]
    me = lax.axis_index("expert")
    expert = me % groups
    named = forward_routes[0][:, :, None] == jnp.arange(groups, dtype=jnp.int32)[None, None, :]
    coef = jnp.sum(jnp.where(named, forward_gates[0][:, :, None], 0.0), axis=1)
    code = coded(coef)
    pad = 128 * ((code.shape[1] + 127) // 128) - code.shape[1]
    code = jnp.pad(code, ((0, 0), (0, pad)))
    col = jnp.concatenate([tokens, code], axis=1)

    col = jnp.stack([col, moved(col, across_z)])
    ring = X_SIZE
    first = jnp.stack([col] + [moved(col, along(0, k)) for k in range(1, ring)])
    second = jnp.stack([first] + [moved(first, along(1, k)) for k in range(1, ring)])
    other = moved(second, across_core)

    mats = (
        jnp.pad(gate_matrix[0, 0], ((0, code.shape[1]), (0, 0))),
        jnp.pad(up_matrix[0, 0], ((0, code.shape[1]), (0, 0))),
        down_matrix[0, 0],
    )
    full = width + code.shape[1]
    own_rows = second.reshape(-1, full)
    own_w = decoded(own_rows[:, width:], groups)[:, expert]
    other_rows = other.reshape(-1, full)
    other_w = decoded(other_rows[:, width:], groups)[:, expert]
    other_part = expert_rows(other_rows, other_w, *mats)
    back = moved(other_part.astype(jnp.bfloat16), across_core)
    own_part = expert_rows(own_rows, own_w, *mats)
    summed = own_part + back.astype(jnp.float32)
    summed = summed.reshape((ring, ring, 2) + tokens.shape)

    total = summed[0]
    sent = summed.astype(jnp.bfloat16)
    for m in range(1, ring):
        total = total + moved(sent[m], along(1, -m)).astype(jnp.float32)
    total_first = total[0]
    sent = total.astype(jnp.bfloat16)
    for k in range(1, ring):
        total_first = total_first + moved(sent[k], along(0, -k)).astype(jnp.float32)
    mine = tokens.astype(jnp.float32) + total_first[0]
    theirs = total_first[1].astype(jnp.bfloat16)
    sections = lax.axis_size("segment")
    count = X_SIZE * Y_SIZE * Z_SIZE * C_SIZE
    relay = [(s * count + e, (s + 1) % sections * count + e) for s in range(sections) for e in range(count)]
    cross = [
        (s * count + e, (s + 1) % sections * count + across_z(*coords(e)))
        for s in range(sections)
        for e in range(count)
    ]
    got_mine = lax.ppermute(mine, ("segment", "expert"), relay)
    got_theirs = lax.ppermute(theirs, ("segment", "expert"), cross)
    next_input = (got_mine + got_theirs.astype(jnp.float32)).astype(jnp.bfloat16)
    return next_input[None]


def solution(mesh):
    in_specs = (
        P("segment", "expert", None),
        P("segment", "expert", None),
        P("segment", "expert", None),
        P("segment", "expert", None, None),
        P("segment", "expert", None, None),
        P("segment", "expert", None, None),
    )
    out_specs = P("segment", "expert", None)
    return jax.shard_map(local, mesh=mesh, in_specs=in_specs, out_specs=out_specs, check_vma=False)
```

```python
import jax
import jax.numpy as jnp
from jax import lax
from jax.sharding import PartitionSpec as P

FH = 1024
X_SIZE, Y_SIZE, Z_SIZE, C_SIZE = 4, 4, 2, 2


def coords(e):
    return (e // (Y_SIZE * Z_SIZE * C_SIZE), (e // (Z_SIZE * C_SIZE)) % Y_SIZE, (e // C_SIZE) % Z_SIZE, e % C_SIZE)


def index_of(x, y, z, c):
    return ((x * Y_SIZE + y) * Z_SIZE + z) * C_SIZE + c


def moved(value, target):
    count = X_SIZE * Y_SIZE * Z_SIZE * C_SIZE
    pairs = [(e, target(*coords(e))) for e in range(count)]
    return lax.ppermute(value, "expert", pairs)


def passed_along(value, axis, steps):
    count = lax.axis_size(axis)
    pairs = [(source, (source + steps) % count) for source in range(count)]
    return lax.ppermute(value, axis, pairs)


def along(axis, step):
    def target(x, y, z, c):
        first = axis if c == 0 else 1 - axis
        if first == 0:
            return index_of((x + step) % X_SIZE, y, z, c)
        return index_of(x, (y + step) % Y_SIZE, z, c)

    return target


def across_z(x, y, z, c):
    return index_of(x, y, 1 - z, c)


def across_core(x, y, z, c):
    return index_of(x, y, z, 1 - c)


def expert_rows(rows, weight, gate_mat, upper_mat, down_mat):
    gate_act = jnp.dot(rows, gate_mat, preferred_element_type=jnp.float32)
    upper_act = jnp.dot(rows, upper_mat, preferred_element_type=jnp.float32)
    hidden = (jax.nn.silu(gate_act) * upper_act).astype(jnp.bfloat16)
    part = jnp.dot(hidden, down_mat, preferred_element_type=jnp.float32)
    return weight[:, None] * part.astype(jnp.bfloat16).astype(jnp.float32)


def coded(coef):
    first = coef.astype(jnp.bfloat16)
    rest = coef - first.astype(jnp.float32)
    second = rest.astype(jnp.bfloat16)
    third = (rest - second.astype(jnp.float32)).astype(jnp.bfloat16)
    return jnp.concatenate([first, second, third], axis=-1)


def decoded(code, groups):
    code = code.astype(jnp.float32)
    return code[..., :groups] + code[..., groups:2 * groups] + code[..., 2 * groups:3 * groups]


def local(forward_input, forward_routes, forward_gates, gate_matrix, up_matrix, down_matrix):
    devices = lax.axis_size("expert")
    hidden_slice = gate_matrix.shape[3]
    split = FH // hidden_slice
    groups = devices // split
    tokens = forward_input[0]
    width = tokens.shape[1]
    me = lax.axis_index("expert")
    expert = me % groups
    named = forward_routes[0][:, :, None] == jnp.arange(groups, dtype=jnp.int32)[None, None, :]
    coef = jnp.sum(jnp.where(named, forward_gates[0][:, :, None], 0.0), axis=1)
    code = coded(coef)
    pad = 128 * ((code.shape[1] + 127) // 128) - code.shape[1]
    code = jnp.pad(code, ((0, 0), (0, pad)))
    col = jnp.concatenate([tokens, code], axis=1)

    mats = (
        jnp.pad(gate_matrix[0, 0], ((0, code.shape[1]), (0, 0))),
        jnp.pad(up_matrix[0, 0], ((0, code.shape[1]), (0, 0))),
        down_matrix[0, 0],
    )
    full = width + code.shape[1]
    ring = X_SIZE

    def served(block):
        first = jnp.stack([block] + [moved(block, along(0, k)) for k in range(1, ring)])
        second = jnp.stack([first] + [moved(first, along(1, k)) for k in range(1, ring)])
        other = moved(second, across_core)
        own_rows = second.reshape(-1, full)
        own_w = decoded(own_rows[:, width:], groups)[:, expert]
        other_rows = other.reshape(-1, full)
        other_w = decoded(other_rows[:, width:], groups)[:, expert]
        other_part = expert_rows(other_rows, other_w, *mats)
        back = moved(other_part.astype(jnp.bfloat16), across_core)
        own_part = expert_rows(own_rows, own_w, *mats)
        summed = own_part + back.astype(jnp.float32)
        summed = summed.reshape((ring, ring) + tokens.shape)
        total = summed[0]
        sent = summed.astype(jnp.bfloat16)
        for m in range(1, ring):
            total = total + moved(sent[m], along(1, -m)).astype(jnp.float32)
        result = total[0]
        sent = total.astype(jnp.bfloat16)
        for k in range(1, ring):
            result = result + moved(sent[k], along(0, -k)).astype(jnp.float32)
        return result

    own_sum = served(col)
    partner_sum = served(moved(col, across_z))

    mine = tokens.astype(jnp.float32) + own_sum
    theirs = partner_sum.astype(jnp.bfloat16)
    sections = lax.axis_size("segment")
    count = X_SIZE * Y_SIZE * Z_SIZE * C_SIZE
    relay = [(s * count + e, (s + 1) % sections * count + e) for s in range(sections) for e in range(count)]
    cross = [
        (s * count + e, (s + 1) % sections * count + across_z(*coords(e)))
        for s in range(sections)
        for e in range(count)
    ]
    got_mine = lax.ppermute(mine, ("segment", "expert"), relay)
    got_theirs = lax.ppermute(theirs, ("segment", "expert"), cross)
    next_input = (got_mine + got_theirs.astype(jnp.float32)).astype(jnp.bfloat16)
    return next_input[None]


def solution(mesh):
    in_specs = (
        P("segment", "expert", None),
        P("segment", "expert", None),
        P("segment", "expert", None),
        P("segment", "expert", None, None),
        P("segment", "expert", None, None),
        P("segment", "expert", None, None),
    )
    out_specs = P("segment", "expert", None)
    return jax.shard_map(local, mesh=mesh, in_specs=in_specs, out_specs=out_specs, check_vma=False)
```

```python
import jax
import jax.numpy as jnp
from jax import lax
from jax.sharding import PartitionSpec as P

FH = 1024
X_SIZE, Y_SIZE, Z_SIZE, C_SIZE = 4, 4, 2, 2


def coords(e):
    return (e // (Y_SIZE * Z_SIZE * C_SIZE), (e // (Z_SIZE * C_SIZE)) % Y_SIZE, (e // C_SIZE) % Z_SIZE, e % C_SIZE)


def index_of(x, y, z, c):
    return ((x * Y_SIZE + y) * Z_SIZE + z) * C_SIZE + c


def moved(value, target):
    count = X_SIZE * Y_SIZE * Z_SIZE * C_SIZE
    pairs = [(e, target(*coords(e))) for e in range(count)]
    return lax.ppermute(value, "expert", pairs)


def passed_along(value, axis, steps):
    count = lax.axis_size(axis)
    pairs = [(source, (source + steps) % count) for source in range(count)]
    return lax.ppermute(value, axis, pairs)


def along(axis, step):
    def target(x, y, z, c):
        first = axis if c == 0 else 1 - axis
        if first == 0:
            return index_of((x + step) % X_SIZE, y, z, c)
        return index_of(x, (y + step) % Y_SIZE, z, c)

    return target


def across_z(x, y, z, c):
    return index_of(x, y, 1 - z, c)


def across_core(x, y, z, c):
    return index_of(x, y, z, 1 - c)


def expert_rows(rows, weight, gate_mat, upper_mat, down_mat):
    gate_act = jnp.dot(rows, gate_mat, preferred_element_type=jnp.float32)
    upper_act = jnp.dot(rows, upper_mat, preferred_element_type=jnp.float32)
    hidden = (jax.nn.silu(gate_act) * upper_act).astype(jnp.bfloat16)
    part = jnp.dot(hidden, down_mat, preferred_element_type=jnp.float32)
    return weight[:, None] * part.astype(jnp.bfloat16).astype(jnp.float32)


def coded(coef):
    first = coef.astype(jnp.bfloat16)
    rest = coef - first.astype(jnp.float32)
    second = rest.astype(jnp.bfloat16)
    third = (rest - second.astype(jnp.float32)).astype(jnp.bfloat16)
    return jnp.concatenate([first, second, third], axis=-1)


def decoded(code, groups):
    code = code.astype(jnp.float32)
    return code[..., :groups] + code[..., groups:2 * groups] + code[..., 2 * groups:3 * groups]


def local(forward_input, forward_routes, forward_gates, gate_matrix, up_matrix, down_matrix):
    devices = lax.axis_size("expert")
    hidden_slice = gate_matrix.shape[3]
    split = FH // hidden_slice
    groups = devices // split
    tokens = forward_input[0]
    width = tokens.shape[1]
    me = lax.axis_index("expert")
    expert = me % groups
    named = forward_routes[0][:, :, None] == jnp.arange(groups, dtype=jnp.int32)[None, None, :]
    coef = jnp.sum(jnp.where(named, forward_gates[0][:, :, None], 0.0), axis=1)
    code = coded(coef)
    pad = 128 * ((code.shape[1] + 127) // 128) - code.shape[1]
    code = jnp.pad(code, ((0, 0), (0, pad)))
    col = jnp.concatenate([tokens, code], axis=1)

    mats = (
        jnp.pad(gate_matrix[0, 0], ((0, code.shape[1]), (0, 0))),
        jnp.pad(up_matrix[0, 0], ((0, code.shape[1]), (0, 0))),
        down_matrix[0, 0],
    )
    full = width + code.shape[1]
    ring = X_SIZE

    def gathered(block):
        first = jnp.stack([block] + [moved(block, along(0, k)) for k in range(1, ring)])
        second = jnp.stack([first] + [moved(first, along(1, k)) for k in range(1, ring)])
        return second, moved(second, across_core)

    own_plane, own_other = gathered(col)
    partner_plane, partner_other = gathered(moved(col, across_z))
    rows = jnp.stack([own_other, partner_other, own_plane, partner_plane]).reshape(-1, full)
    weight = decoded(rows[:, width:], groups)[:, expert]
    part = expert_rows(rows, weight, *mats)
    half = part.shape[0] // 2
    back = moved(part[:half].astype(jnp.bfloat16), across_core)
    summed = part[half:] + back.astype(jnp.float32)
    summed = summed.reshape((2, ring, ring) + tokens.shape)
    total = summed[:, 0]
    sent = summed.astype(jnp.bfloat16)
    for m in range(1, ring):
        total = total + moved(sent[:, m], along(1, -m)).astype(jnp.float32)
    result = total[:, 0]
    sent = total.astype(jnp.bfloat16)
    for k in range(1, ring):
        result = result + moved(sent[:, k], along(0, -k)).astype(jnp.float32)
    own_sum, partner_sum = result[0], result[1]

    mine = tokens.astype(jnp.float32) + own_sum
    theirs = partner_sum.astype(jnp.bfloat16)
    sections = lax.axis_size("segment")
    count = X_SIZE * Y_SIZE * Z_SIZE * C_SIZE
    relay = [(s * count + e, (s + 1) % sections * count + e) for s in range(sections) for e in range(count)]
    cross = [
        (s * count + e, (s + 1) % sections * count + across_z(*coords(e)))
        for s in range(sections)
        for e in range(count)
    ]
    got_mine = lax.ppermute(mine, ("segment", "expert"), relay)
    got_theirs = lax.ppermute(theirs, ("segment", "expert"), cross)
    next_input = (got_mine + got_theirs.astype(jnp.float32)).astype(jnp.bfloat16)
    return next_input[None]


def solution(mesh):
    in_specs = (
        P("segment", "expert", None),
        P("segment", "expert", None),
        P("segment", "expert", None),
        P("segment", "expert", None, None),
        P("segment", "expert", None, None),
        P("segment", "expert", None, None),
    )
    out_specs = P("segment", "expert", None)
    return jax.shard_map(local, mesh=mesh, in_specs=in_specs, out_specs=out_specs, check_vma=False)
```

```python
import jax
import jax.numpy as jnp
from jax import lax
from jax.sharding import PartitionSpec as P

FH = 1024
X_SIZE, Y_SIZE, Z_SIZE, C_SIZE = 4, 4, 2, 2


def coords(e):
    return (e // (Y_SIZE * Z_SIZE * C_SIZE), (e // (Z_SIZE * C_SIZE)) % Y_SIZE, (e // C_SIZE) % Z_SIZE, e % C_SIZE)


def index_of(x, y, z, c):
    return ((x * Y_SIZE + y) * Z_SIZE + z) * C_SIZE + c


def moved(value, target):
    count = X_SIZE * Y_SIZE * Z_SIZE * C_SIZE
    pairs = [(e, target(*coords(e))) for e in range(count)]
    return lax.ppermute(value, "expert", pairs)


def passed_along(value, axis, steps):
    count = lax.axis_size(axis)
    pairs = [(source, (source + steps) % count) for source in range(count)]
    return lax.ppermute(value, axis, pairs)


def along(axis, step):
    def target(x, y, z, c):
        first = axis if c == 0 else 1 - axis
        if first == 0:
            return index_of((x + step) % X_SIZE, y, z, c)
        return index_of(x, (y + step) % Y_SIZE, z, c)

    return target


def ring_gather(block, axis, split, join):
    from_back = moved(block, along(axis, 1))
    from_front = moved(block, along(axis, -1))
    far_a = moved(split(from_back)[0], along(axis, 1))
    far_b = moved(split(from_front)[1], along(axis, -1))
    return jnp.stack([block, from_back, join(far_a, far_b), from_front])


def ring_reduce(parts, axis, split, join):
    far_a, far_b = split(parts[2].astype(jnp.bfloat16))
    got_a = moved(far_a, along(axis, -1)).astype(jnp.float32)
    got_b = moved(far_b, along(axis, 1)).astype(jnp.float32)
    near_a, near_b = split(parts[1])
    to_front = join(near_a + got_a, near_b).astype(jnp.bfloat16)
    back_a, back_b = split(parts[3])
    to_back = join(back_a, back_b + got_b).astype(jnp.bfloat16)
    return (
        parts[0]
        + moved(to_front, along(axis, -1)).astype(jnp.float32)
        + moved(to_back, along(axis, 1)).astype(jnp.float32)
    )


def halves(axis, at):
    def split(value):
        return lax.slice_in_dim(value, 0, at, axis=axis), lax.slice_in_dim(value, at, value.shape[axis], axis=axis)

    def join(first, second):
        return jnp.concatenate([first, second], axis=axis)

    return split, join


def across_z(x, y, z, c):
    return index_of(x, y, 1 - z, c)


def across_core(x, y, z, c):
    return index_of(x, y, z, 1 - c)


def expert_rows(rows, weight, gate_mat, upper_mat, down_mat):
    gate_act = jnp.dot(rows, gate_mat, preferred_element_type=jnp.float32)
    upper_act = jnp.dot(rows, upper_mat, preferred_element_type=jnp.float32)
    hidden = (jax.nn.silu(gate_act) * upper_act).astype(jnp.bfloat16)
    part = jnp.dot(hidden, down_mat, preferred_element_type=jnp.float32)
    return weight[:, None] * part.astype(jnp.bfloat16).astype(jnp.float32)


def coded(coef):
    first = coef.astype(jnp.bfloat16)
    rest = coef - first.astype(jnp.float32)
    second = rest.astype(jnp.bfloat16)
    third = (rest - second.astype(jnp.float32)).astype(jnp.bfloat16)
    return jnp.concatenate([first, second, third], axis=-1)


def decoded(code, groups):
    code = code.astype(jnp.float32)
    return code[..., :groups] + code[..., groups:2 * groups] + code[..., 2 * groups:3 * groups]


def local(forward_input, forward_routes, forward_gates, gate_matrix, up_matrix, down_matrix):
    devices = lax.axis_size("expert")
    hidden_slice = gate_matrix.shape[3]
    split = FH // hidden_slice
    groups = devices // split
    tokens = forward_input[0]
    width = tokens.shape[1]
    me = lax.axis_index("expert")
    expert = me % groups
    named = forward_routes[0][:, :, None] == jnp.arange(groups, dtype=jnp.int32)[None, None, :]
    coef = jnp.sum(jnp.where(named, forward_gates[0][:, :, None], 0.0), axis=1)
    code = coded(coef)
    pad = 128 * ((code.shape[1] + 127) // 128) - code.shape[1]
    code = jnp.pad(code, ((0, 0), (0, pad)))
    col = jnp.concatenate([tokens, code], axis=1)

    mats = (
        jnp.pad(gate_matrix[0, 0], ((0, code.shape[1]), (0, 0))),
        jnp.pad(up_matrix[0, 0], ((0, code.shape[1]), (0, 0))),
        down_matrix[0, 0],
    )
    full = width + code.shape[1]
    ring = X_SIZE

    def gathered(block):
        first = ring_gather(block, 0, *halves(1, width // 2))
        second = ring_gather(first, 1, *halves(0, ring // 2))
        return second, moved(second, across_core)

    own_plane, own_other = gathered(col)
    partner_plane, partner_other = gathered(moved(col, across_z))
    rows = jnp.stack([own_other, partner_other, own_plane, partner_plane]).reshape(-1, full)
    weight = decoded(rows[:, width:], groups)[:, expert]
    part = expert_rows(rows, weight, *mats)
    half = part.shape[0] // 2
    back = moved(part[:half].astype(jnp.bfloat16), across_core)
    summed = part[half:] + back.astype(jnp.float32)
    summed = summed.reshape((2, ring, ring) + tokens.shape)
    total = ring_reduce([summed[:, m] for m in range(ring)], 1, *halves(1, ring // 2))
    result = ring_reduce([total[:, k] for k in range(ring)], 0, *halves(0, 1))
    own_sum, partner_sum = result[0], result[1]

    mine = tokens.astype(jnp.float32) + own_sum
    theirs = partner_sum.astype(jnp.bfloat16)
    sections = lax.axis_size("segment")
    count = X_SIZE * Y_SIZE * Z_SIZE * C_SIZE
    relay = [(s * count + e, (s + 1) % sections * count + e) for s in range(sections) for e in range(count)]
    cross = [
        (s * count + e, (s + 1) % sections * count + across_z(*coords(e)))
        for s in range(sections)
        for e in range(count)
    ]
    got_mine = lax.ppermute(mine, ("segment", "expert"), relay)
    got_theirs = lax.ppermute(theirs, ("segment", "expert"), cross)
    next_input = (got_mine + got_theirs.astype(jnp.float32)).astype(jnp.bfloat16)
    return next_input[None]


def solution(mesh):
    in_specs = (
        P("segment", "expert", None),
        P("segment", "expert", None),
        P("segment", "expert", None),
        P("segment", "expert", None, None),
        P("segment", "expert", None, None),
        P("segment", "expert", None, None),
    )
    out_specs = P("segment", "expert", None)
    return jax.shard_map(local, mesh=mesh, in_specs=in_specs, out_specs=out_specs, check_vma=False)
```

```python
import jax
import jax.numpy as jnp
from jax import lax
from jax.sharding import PartitionSpec as P

FH = 1024
X_SIZE, Y_SIZE, Z_SIZE, C_SIZE = 4, 4, 2, 2


def coords(e):
    return (e // (Y_SIZE * Z_SIZE * C_SIZE), (e // (Z_SIZE * C_SIZE)) % Y_SIZE, (e // C_SIZE) % Z_SIZE, e % C_SIZE)


def index_of(x, y, z, c):
    return ((x * Y_SIZE + y) * Z_SIZE + z) * C_SIZE + c


def moved(value, target):
    count = X_SIZE * Y_SIZE * Z_SIZE * C_SIZE
    pairs = [(e, target(*coords(e))) for e in range(count)]
    return lax.ppermute(value, "expert", pairs)


def passed_along(value, axis, steps):
    count = lax.axis_size(axis)
    pairs = [(source, (source + steps) % count) for source in range(count)]
    return lax.ppermute(value, axis, pairs)


def along(axis, step):
    def target(x, y, z, c):
        first = axis if c == 0 else 1 - axis
        if first == 0:
            return index_of((x + step) % X_SIZE, y, z, c)
        return index_of(x, (y + step) % Y_SIZE, z, c)

    return target


def across_z(x, y, z, c):
    return index_of(x, y, 1 - z, c)


def across_core(x, y, z, c):
    return index_of(x, y, z, 1 - c)


def expert_rows(rows, weight, gate_mat, upper_mat, down_mat):
    gate_act = jnp.dot(rows, gate_mat, preferred_element_type=jnp.float32)
    upper_act = jnp.dot(rows, upper_mat, preferred_element_type=jnp.float32)
    hidden = (jax.nn.silu(gate_act) * upper_act).astype(jnp.bfloat16)
    part = jnp.dot(hidden, down_mat, preferred_element_type=jnp.float32)
    return weight[:, None] * part.astype(jnp.bfloat16).astype(jnp.float32)


def coded(coef):
    first = coef.astype(jnp.bfloat16)
    rest = coef - first.astype(jnp.float32)
    second = rest.astype(jnp.bfloat16)
    third = (rest - second.astype(jnp.float32)).astype(jnp.bfloat16)
    return jnp.concatenate([first, second, third], axis=-1)


def decoded(code, groups):
    code = code.astype(jnp.float32)
    return code[..., :groups] + code[..., groups:2 * groups] + code[..., 2 * groups:3 * groups]


def local(forward_input, forward_routes, forward_gates, gate_matrix, up_matrix, down_matrix):
    devices = lax.axis_size("expert")
    hidden_slice = gate_matrix.shape[3]
    split = FH // hidden_slice
    groups = devices // split
    tokens = forward_input[0]
    width = tokens.shape[1]
    me = lax.axis_index("expert")
    expert = me % groups
    named = forward_routes[0][:, :, None] == jnp.arange(groups, dtype=jnp.int32)[None, None, :]
    coef = jnp.sum(jnp.where(named, forward_gates[0][:, :, None], 0.0), axis=1)
    code = coded(coef)
    pad = 128 * ((code.shape[1] + 127) // 128) - code.shape[1]
    code = jnp.pad(code, ((0, 0), (0, pad)))
    col = jnp.concatenate([tokens, code], axis=1)

    mats = (
        jnp.pad(gate_matrix[0, 0], ((0, code.shape[1]), (0, 0))),
        jnp.pad(up_matrix[0, 0], ((0, code.shape[1]), (0, 0))),
        down_matrix[0, 0],
    )
    full = width + code.shape[1]
    ring = X_SIZE

    def served(block):
        first = jnp.stack([block] + [moved(block, along(0, k)) for k in range(1, ring)])
        second = jnp.stack([first] + [moved(first, along(1, k)) for k in range(1, ring)])
        other = moved(second, across_core)
        rows = jnp.stack([other, second]).reshape(-1, full)
        weight = decoded(rows[:, width:], groups)[:, expert]
        part = expert_rows(rows, weight, *mats).astype(jnp.bfloat16)
        half = part.shape[0] // 2
        back = moved(part[:half], across_core)
        summed = part[half:].astype(jnp.float32) + back.astype(jnp.float32)
        summed = summed.reshape((ring, ring) + tokens.shape)
        total = summed[0]
        sent = summed.astype(jnp.bfloat16)
        for m in range(1, ring):
            total = total + moved(sent[m], along(1, -m)).astype(jnp.float32)
        result = total[0]
        sent = total.astype(jnp.bfloat16)
        for k in range(1, ring):
            result = result + moved(sent[k], along(0, -k)).astype(jnp.float32)
        return result

    own_sum = served(col)
    partner_sum = served(moved(col, across_z))

    mine = tokens.astype(jnp.float32) + own_sum
    theirs = partner_sum.astype(jnp.bfloat16)
    sections = lax.axis_size("segment")
    count = X_SIZE * Y_SIZE * Z_SIZE * C_SIZE
    relay = [(s * count + e, (s + 1) % sections * count + e) for s in range(sections) for e in range(count)]
    cross = [
        (s * count + e, (s + 1) % sections * count + across_z(*coords(e)))
        for s in range(sections)
        for e in range(count)
    ]
    got_mine = lax.ppermute(mine, ("segment", "expert"), relay)
    got_theirs = lax.ppermute(theirs, ("segment", "expert"), cross)
    next_input = (got_mine + got_theirs.astype(jnp.float32)).astype(jnp.bfloat16)
    return next_input[None]


def solution(mesh):
    in_specs = (
        P("segment", "expert", None),
        P("segment", "expert", None),
        P("segment", "expert", None),
        P("segment", "expert", None, None),
        P("segment", "expert", None, None),
        P("segment", "expert", None, None),
    )
    out_specs = P("segment", "expert", None)
    return jax.shard_map(local, mesh=mesh, in_specs=in_specs, out_specs=out_specs, check_vma=False)
```

```python
import jax
import jax.numpy as jnp
from jax import lax
from jax.sharding import PartitionSpec as P

FH = 1024
X_SIZE, Y_SIZE, Z_SIZE, C_SIZE = 4, 4, 2, 2


def coords(e):
    return (e // (Y_SIZE * Z_SIZE * C_SIZE), (e // (Z_SIZE * C_SIZE)) % Y_SIZE, (e // C_SIZE) % Z_SIZE, e % C_SIZE)


def index_of(x, y, z, c):
    return ((x * Y_SIZE + y) * Z_SIZE + z) * C_SIZE + c


def moved(value, target):
    count = X_SIZE * Y_SIZE * Z_SIZE * C_SIZE
    pairs = [(e, target(*coords(e))) for e in range(count)]
    return lax.ppermute(value, "expert", pairs)


def along(axis, step):
    def target(x, y, z, c):
        first = axis if c == 0 else 1 - axis
        if first == 0:
            return index_of((x + step) % X_SIZE, y, z, c)
        return index_of(x, (y + step) % Y_SIZE, z, c)

    return target


def across_z(x, y, z, c):
    return index_of(x, y, 1 - z, c)


def across_core(x, y, z, c):
    return index_of(x, y, z, 1 - c)


def expert_rows(rows, weight, gate_mat, upper_mat, down_mat):
    gate_act = jnp.dot(rows, gate_mat, preferred_element_type=jnp.float32)
    upper_act = jnp.dot(rows, upper_mat, preferred_element_type=jnp.float32)
    hidden = (jax.nn.silu(gate_act) * upper_act).astype(jnp.bfloat16)
    part = jnp.dot(hidden, down_mat, preferred_element_type=jnp.float32)
    return weight[:, None] * part.astype(jnp.bfloat16).astype(jnp.float32)


def coded(coef):
    first = coef.astype(jnp.bfloat16)
    rest = coef - first.astype(jnp.float32)
    second = rest.astype(jnp.bfloat16)
    third = (rest - second.astype(jnp.float32)).astype(jnp.bfloat16)
    return jnp.concatenate([first, second, third], axis=-1)


def decoded(code, groups):
    code = code.astype(jnp.float32)
    return code[..., :groups] + code[..., groups:2 * groups] + code[..., 2 * groups:3 * groups]


def layer(forward_input, forward_routes, forward_gates, gate_matrix, up_matrix, down_matrix):
    devices = lax.axis_size("expert")
    hidden_slice = gate_matrix.shape[3]
    split = FH // hidden_slice
    groups = devices // split
    tokens = forward_input[0]
    width = tokens.shape[1]
    me = lax.axis_index("expert")
    expert = me % groups
    named = forward_routes[0][:, :, None] == jnp.arange(groups, dtype=jnp.int32)[None, None, :]
    coef = jnp.sum(jnp.where(named, forward_gates[0][:, :, None], 0.0), axis=1)
    code = coded(coef)
    pad = 128 * ((code.shape[1] + 127) // 128) - code.shape[1]
    code = jnp.pad(code, ((0, 0), (0, pad)))
    col = jnp.concatenate([tokens, code], axis=1)

    mats = (
        jnp.pad(gate_matrix[0, 0], ((0, code.shape[1]), (0, 0))),
        jnp.pad(up_matrix[0, 0], ((0, code.shape[1]), (0, 0))),
        down_matrix[0, 0],
    )
    full = width + code.shape[1]
    ring = X_SIZE

    def served(block):
        first = jnp.stack([block] + [moved(block, along(0, k)) for k in range(1, ring)])
        second = jnp.stack([first] + [moved(first, along(1, k)) for k in range(1, ring)])
        other = moved(second, across_core)
        rows = jnp.stack([other, second]).reshape(-1, full)
        weight = decoded(rows[:, width:], groups)[:, expert]
        part = expert_rows(rows, weight, *mats).astype(jnp.bfloat16)
        half = part.shape[0] // 2
        back = moved(part[:half], across_core)
        summed = part[half:].astype(jnp.float32) + back.astype(jnp.float32)
        summed = summed.reshape((ring, ring) + tokens.shape)
        total = summed[0]
        sent = summed.astype(jnp.bfloat16)
        for m in range(1, ring):
            total = total + moved(sent[m], along(1, -m)).astype(jnp.float32)
        result = total[0]
        sent = total.astype(jnp.bfloat16)
        for k in range(1, ring):
            result = result + moved(sent[k], along(0, -k)).astype(jnp.float32)
        return result

    own_sum = served(col)
    partner_sum = served(moved(col, across_z))

    mine = tokens.astype(jnp.float32) + own_sum
    theirs = partner_sum.astype(jnp.bfloat16)
    sections = lax.axis_size("segment")
    count = X_SIZE * Y_SIZE * Z_SIZE * C_SIZE
    relay = [(s * count + e, (s + 1) % sections * count + e) for s in range(sections) for e in range(count)]
    cross = [
        (s * count + e, (s + 1) % sections * count + across_z(*coords(e)))
        for s in range(sections)
        for e in range(count)
    ]
    got_mine = lax.ppermute(mine, ("segment", "expert"), relay)
    got_theirs = lax.ppermute(theirs, ("segment", "expert"), cross)
    next_input = (got_mine + got_theirs.astype(jnp.float32)).astype(jnp.bfloat16)
    return next_input[None]


def solution(mesh):
    in_specs = (
        P("segment", "expert", None),
        P("segment", "expert", None),
        P("segment", "expert", None),
        P("segment", "expert", None, None),
        P("segment", "expert", None, None),
        P("segment", "expert", None, None),
    )
    out_specs = P("segment", "expert", None)
    return jax.shard_map(layer, mesh=mesh, in_specs=in_specs, out_specs=out_specs, check_vma=False)
```

```python
import jax
import jax.numpy as jnp
from jax import lax
from jax.sharding import PartitionSpec as P

FH = 1024
X_SIZE, Y_SIZE, Z_SIZE, C_SIZE = 4, 4, 2, 2


def coords(e):
    return (e // (Y_SIZE * Z_SIZE * C_SIZE), (e // (Z_SIZE * C_SIZE)) % Y_SIZE, (e // C_SIZE) % Z_SIZE, e % C_SIZE)


def index_of(x, y, z, c):
    return ((x * Y_SIZE + y) * Z_SIZE + z) * C_SIZE + c


def moved(value, target):
    count = X_SIZE * Y_SIZE * Z_SIZE * C_SIZE
    pairs = [(e, target(*coords(e))) for e in range(count)]
    return lax.ppermute(value, "expert", pairs)


def along(axis, step):
    def target(x, y, z, c):
        first = axis if c == 0 else 1 - axis
        if first == 0:
            return index_of((x + step) % X_SIZE, y, z, c)
        return index_of(x, (y + step) % Y_SIZE, z, c)

    return target


def across_z(x, y, z, c):
    return index_of(x, y, 1 - z, c)


def across_core(x, y, z, c):
    return index_of(x, y, z, 1 - c)


def expert_rows(rows, weight, gate_mat, upper_mat, down_mat):
    gate_act = jnp.dot(rows, gate_mat, preferred_element_type=jnp.float32)
    upper_act = jnp.dot(rows, upper_mat, preferred_element_type=jnp.float32)
    hidden = (jax.nn.silu(gate_act) * upper_act).astype(jnp.bfloat16)
    part = jnp.dot(hidden, down_mat, preferred_element_type=jnp.float32)
    return weight[:, None] * part.astype(jnp.bfloat16).astype(jnp.float32)


def coded(coef):
    first = coef.astype(jnp.bfloat16)
    rest = coef - first.astype(jnp.float32)
    second = rest.astype(jnp.bfloat16)
    third = (rest - second.astype(jnp.float32)).astype(jnp.bfloat16)
    return jnp.concatenate([first, second, third], axis=-1)


def decoded(code, groups):
    code = code.astype(jnp.float32)
    return code[..., :groups] + code[..., groups:2 * groups] + code[..., 2 * groups:3 * groups]


def layer(forward_input, forward_routes, forward_gates, gate_matrix, up_matrix, down_matrix):
    devices = lax.axis_size("expert")
    hidden_slice = gate_matrix.shape[3]
    split = FH // hidden_slice
    groups = devices // split
    tokens = forward_input[0]
    width = tokens.shape[1]
    me = lax.axis_index("expert")
    expert = me % groups
    named = forward_routes[0][:, :, None] == jnp.arange(groups, dtype=jnp.int32)[None, None, :]
    coef = jnp.sum(jnp.where(named, forward_gates[0][:, :, None], 0.0), axis=1)
    code = coded(coef)
    pad = 128 * ((code.shape[1] + 127) // 128) - code.shape[1]
    code = jnp.pad(code, ((0, 0), (0, pad)))
    col = jnp.concatenate([tokens, code], axis=1)

    mats = (
        jnp.pad(gate_matrix[0, 0], ((0, code.shape[1]), (0, 0))),
        jnp.pad(up_matrix[0, 0], ((0, code.shape[1]), (0, 0))),
        down_matrix[0, 0],
    )
    full = width + code.shape[1]
    ring = X_SIZE

    def served(block, after=None):
        first = jnp.stack([block] + [moved(block, along(0, k)) for k in range(1, ring)])
        second = jnp.stack([first] + [moved(first, along(1, k)) for k in range(1, ring)])
        other = moved(second, across_core)
        rows = jnp.stack([other, second]).reshape(-1, full)
        if after is not None:
            rows, _ = lax.optimization_barrier((rows, after))
        weight = decoded(rows[:, width:], groups)[:, expert]
        part = expert_rows(rows, weight, *mats).astype(jnp.bfloat16)
        half = part.shape[0] // 2
        back = moved(part[:half], across_core)
        summed = part[half:].astype(jnp.float32) + back.astype(jnp.float32)
        summed = summed.reshape((ring, ring) + tokens.shape)
        total = summed[0]
        sent = summed.astype(jnp.bfloat16)
        for m in range(1, ring):
            total = total + moved(sent[m], along(1, -m)).astype(jnp.float32)
        result = total[0]
        sent = total.astype(jnp.bfloat16)
        for k in range(1, ring):
            result = result + moved(sent[k], along(0, -k)).astype(jnp.float32)
        return result, part

    own_sum, first_part = served(col)
    partner_sum, _ = served(moved(col, across_z), first_part)

    mine = tokens.astype(jnp.float32) + own_sum
    theirs = partner_sum.astype(jnp.bfloat16)
    sections = lax.axis_size("segment")
    count = X_SIZE * Y_SIZE * Z_SIZE * C_SIZE
    relay = [(s * count + e, (s + 1) % sections * count + e) for s in range(sections) for e in range(count)]
    cross = [
        (s * count + e, (s + 1) % sections * count + across_z(*coords(e)))
        for s in range(sections)
        for e in range(count)
    ]
    got_mine = lax.ppermute(mine, ("segment", "expert"), relay)
    got_theirs = lax.ppermute(theirs, ("segment", "expert"), cross)
    next_input = (got_mine + got_theirs.astype(jnp.float32)).astype(jnp.bfloat16)
    return next_input[None]


def solution(mesh):
    in_specs = (
        P("segment", "expert", None),
        P("segment", "expert", None),
        P("segment", "expert", None),
        P("segment", "expert", None, None),
        P("segment", "expert", None, None),
        P("segment", "expert", None, None),
    )
    out_specs = P("segment", "expert", None)
    return jax.shard_map(layer, mesh=mesh, in_specs=in_specs, out_specs=out_specs, check_vma=False)
```

```python
import jax
import jax.numpy as jnp
from jax import lax
from jax.sharding import PartitionSpec as P

FH = 1024
X_SIZE, Y_SIZE, Z_SIZE, C_SIZE = 4, 4, 2, 2


def coords(e):
    return (e // (Y_SIZE * Z_SIZE * C_SIZE), (e // (Z_SIZE * C_SIZE)) % Y_SIZE, (e // C_SIZE) % Z_SIZE, e % C_SIZE)


def index_of(x, y, z, c):
    return ((x * Y_SIZE + y) * Z_SIZE + z) * C_SIZE + c


def moved(value, target):
    count = X_SIZE * Y_SIZE * Z_SIZE * C_SIZE
    pairs = [(e, target(*coords(e))) for e in range(count)]
    return lax.ppermute(value, "expert", pairs)


def along(axis, step):
    def target(x, y, z, c):
        first = axis if c == 0 else 1 - axis
        if first == 0:
            return index_of((x + step) % X_SIZE, y, z, c)
        return index_of(x, (y + step) % Y_SIZE, z, c)

    return target


def across_z(x, y, z, c):
    return index_of(x, y, 1 - z, c)


def across_core(x, y, z, c):
    return index_of(x, y, z, 1 - c)


def expert_rows(rows, weight, gate_mat, upper_mat, down_mat):
    gate_act = jnp.dot(rows, gate_mat, preferred_element_type=jnp.float32)
    upper_act = jnp.dot(rows, upper_mat, preferred_element_type=jnp.float32)
    hidden = (jax.nn.silu(gate_act) * upper_act).astype(jnp.bfloat16)
    part = jnp.dot(hidden, down_mat, preferred_element_type=jnp.float32)
    return weight[:, None] * part.astype(jnp.bfloat16).astype(jnp.float32)


def coded(coef):
    first = coef.astype(jnp.bfloat16)
    rest = coef - first.astype(jnp.float32)
    second = rest.astype(jnp.bfloat16)
    third = (rest - second.astype(jnp.float32)).astype(jnp.bfloat16)
    return jnp.concatenate([first, second, third], axis=-1)


def decoded(code, groups):
    code = code.astype(jnp.float32)
    return code[..., :groups] + code[..., groups:2 * groups] + code[..., 2 * groups:3 * groups]


def layer(forward_input, forward_routes, forward_gates, gate_matrix, up_matrix, down_matrix):
    devices = lax.axis_size("expert")
    hidden_slice = gate_matrix.shape[3]
    split = FH // hidden_slice
    groups = devices // split
    tokens = forward_input[0]
    width = tokens.shape[1]
    me = lax.axis_index("expert")
    expert = me % groups
    named = forward_routes[0][:, :, None] == jnp.arange(groups, dtype=jnp.int32)[None, None, :]
    coef = jnp.sum(jnp.where(named, forward_gates[0][:, :, None], 0.0), axis=1)
    code = coded(coef)
    pad = 128 * ((code.shape[1] + 127) // 128) - code.shape[1]
    code = jnp.pad(code, ((0, 0), (0, pad)))
    col = jnp.concatenate([tokens, code], axis=1)

    mats = (
        jnp.pad(gate_matrix[0, 0], ((0, code.shape[1]), (0, 0))),
        jnp.pad(up_matrix[0, 0], ((0, code.shape[1]), (0, 0))),
        down_matrix[0, 0],
    )
    full = width + code.shape[1]
    ring = X_SIZE

    def served(block, after=None):
        first = jnp.stack([block] + [moved(block, along(0, k)) for k in range(1, ring)])
        second = jnp.stack([first] + [moved(first, along(1, k)) for k in range(1, ring)])
        other = moved(second, across_core)
        rows = jnp.stack([other, second]).reshape(-1, full)
        codes = rows[:, width:]
        if after is not None:
            codes, _ = lax.optimization_barrier((codes, after))
        weight = decoded(codes, groups)[:, expert]
        part = expert_rows(rows, weight, *mats).astype(jnp.bfloat16)
        half = part.shape[0] // 2
        back = moved(part[:half], across_core)
        summed = part[half:].astype(jnp.float32) + back.astype(jnp.float32)
        summed = summed.reshape((ring, ring) + tokens.shape)
        total = summed[0]
        sent = summed.astype(jnp.bfloat16)
        for m in range(1, ring):
            total = total + moved(sent[m], along(1, -m)).astype(jnp.float32)
        result = total[0]
        sent = total.astype(jnp.bfloat16)
        for k in range(1, ring):
            result = result + moved(sent[k], along(0, -k)).astype(jnp.float32)
        return result, part

    partner_col = moved(col, across_z)
    own_sum, first_part = served(col)
    partner_sum, _ = served(partner_col, first_part)

    mine = tokens.astype(jnp.float32) + own_sum
    theirs = partner_sum.astype(jnp.bfloat16)
    sections = lax.axis_size("segment")
    count = X_SIZE * Y_SIZE * Z_SIZE * C_SIZE
    relay = [(s * count + e, (s + 1) % sections * count + e) for s in range(sections) for e in range(count)]
    cross = [
        (s * count + e, (s + 1) % sections * count + across_z(*coords(e)))
        for s in range(sections)
        for e in range(count)
    ]
    got_mine = lax.ppermute(mine, ("segment", "expert"), relay)
    got_theirs = lax.ppermute(theirs, ("segment", "expert"), cross)
    next_input = (got_mine + got_theirs.astype(jnp.float32)).astype(jnp.bfloat16)
    return next_input[None]


def solution(mesh):
    in_specs = (
        P("segment", "expert", None),
        P("segment", "expert", None),
        P("segment", "expert", None),
        P("segment", "expert", None, None),
        P("segment", "expert", None, None),
        P("segment", "expert", None, None),
    )
    out_specs = P("segment", "expert", None)
    return jax.shard_map(layer, mesh=mesh, in_specs=in_specs, out_specs=out_specs, check_vma=False)
```

```python
import jax
import jax.numpy as jnp
from jax import lax
from jax.sharding import PartitionSpec as P

FH = 1024
X_SIZE, Y_SIZE, Z_SIZE, C_SIZE = 4, 4, 2, 2


def coords(e):
    return (e // (Y_SIZE * Z_SIZE * C_SIZE), (e // (Z_SIZE * C_SIZE)) % Y_SIZE, (e // C_SIZE) % Z_SIZE, e % C_SIZE)


def index_of(x, y, z, c):
    return ((x * Y_SIZE + y) * Z_SIZE + z) * C_SIZE + c


def moved(value, target):
    count = X_SIZE * Y_SIZE * Z_SIZE * C_SIZE
    pairs = [(e, target(*coords(e))) for e in range(count)]
    return lax.ppermute(value, "expert", pairs)


def along(axis, step):
    def target(x, y, z, c):
        first = axis if c == 0 else 1 - axis
        if first == 0:
            return index_of((x + step) % X_SIZE, y, z, c)
        return index_of(x, (y + step) % Y_SIZE, z, c)

    return target


def across_z(x, y, z, c):
    return index_of(x, y, 1 - z, c)


def across_core(x, y, z, c):
    return index_of(x, y, z, 1 - c)


def expert_rows(rows, weight, gate_mat, upper_mat, down_mat):
    gate_act = jnp.dot(rows, gate_mat, preferred_element_type=jnp.float32)
    upper_act = jnp.dot(rows, upper_mat, preferred_element_type=jnp.float32)
    hidden = (jax.nn.silu(gate_act) * upper_act).astype(jnp.bfloat16)
    part = jnp.dot(hidden, down_mat, preferred_element_type=jnp.float32)
    return weight[:, None] * part.astype(jnp.bfloat16).astype(jnp.float32)


def coded(coef):
    first = coef.astype(jnp.bfloat16)
    rest = coef - first.astype(jnp.float32)
    second = rest.astype(jnp.bfloat16)
    third = (rest - second.astype(jnp.float32)).astype(jnp.bfloat16)
    return jnp.concatenate([first, second, third], axis=-1)


def decoded(code, groups):
    code = code.astype(jnp.float32)
    return code[..., :groups] + code[..., groups:2 * groups] + code[..., 2 * groups:3 * groups]


def layer(forward_input, forward_routes, forward_gates, gate_matrix, up_matrix, down_matrix):
    devices = lax.axis_size("expert")
    hidden_slice = gate_matrix.shape[3]
    split = FH // hidden_slice
    groups = devices // split
    tokens = forward_input[0]
    width = tokens.shape[1]
    me = lax.axis_index("expert")
    expert = me % groups
    named = forward_routes[0][:, :, None] == jnp.arange(groups, dtype=jnp.int32)[None, None, :]
    coef = jnp.sum(jnp.where(named, forward_gates[0][:, :, None], 0.0), axis=1)
    code = coded(coef)
    pad = 128 * ((code.shape[1] + 127) // 128) - code.shape[1]
    code = jnp.pad(code, ((0, 0), (0, pad)))
    col = jnp.concatenate([tokens, code], axis=1)

    mats = (
        jnp.pad(gate_matrix[0, 0], ((0, code.shape[1]), (0, 0))),
        jnp.pad(up_matrix[0, 0], ((0, code.shape[1]), (0, 0))),
        down_matrix[0, 0],
    )
    full = width + code.shape[1]
    ring = X_SIZE

    def served(block, after=None):
        first = jnp.stack([block] + [moved(block, along(0, k)) for k in range(1, ring)])
        second = jnp.stack([first] + [moved(first, along(1, k)) for k in range(1, ring)])
        other = moved(second, across_core)
        rows = jnp.stack([other, second]).reshape(-1, full)
        codes = rows[:, width:]
        if after is not None:
            codes, _ = lax.optimization_barrier((codes, after))
        weight = decoded(codes, groups)[:, expert]
        part = expert_rows(rows, weight, *mats).astype(jnp.bfloat16)
        half = part.shape[0] // 2
        back = moved(part[:half], across_core)
        summed = part[half:].astype(jnp.float32) + back.astype(jnp.float32)
        summed = summed.reshape((ring, ring) + tokens.shape)
        total = summed[0]
        sent = summed.astype(jnp.bfloat16)
        for m in range(1, ring):
            total = total + moved(sent[m], along(1, -m)).astype(jnp.float32)
        if after is not None:
            return total, part
        result = total[0]
        sent = total.astype(jnp.bfloat16)
        for k in range(1, ring):
            result = result + moved(sent[k], along(0, -k)).astype(jnp.float32)
        return result, part

    partner_col = moved(col, across_z)
    own_sum, first_part = served(col)
    partner_sum, _ = served(partner_col, first_part)

    mine = tokens.astype(jnp.float32) + own_sum
    theirs = partner_sum.astype(jnp.bfloat16)
    ahead_of = lambda k: (lambda e: across_z(*coords(along(0, -k)(*coords(e)))))
    sections = lax.axis_size("segment")
    count = X_SIZE * Y_SIZE * Z_SIZE * C_SIZE
    relay = [(s * count + e, (s + 1) % sections * count + e) for s in range(sections) for e in range(count)]
    got_mine = lax.ppermute(mine, ("segment", "expert"), relay)
    got = got_mine
    for k in range(ring):
        pairs = [
            (s * count + e, (s + 1) % sections * count + ahead_of(k)(e))
            for s in range(sections)
            for e in range(count)
        ]
        got = got + lax.ppermute(theirs[k], ("segment", "expert"), pairs).astype(jnp.float32)
    next_input = got.astype(jnp.bfloat16)
    return next_input[None]


def solution(mesh):
    in_specs = (
        P("segment", "expert", None),
        P("segment", "expert", None),
        P("segment", "expert", None),
        P("segment", "expert", None, None),
        P("segment", "expert", None, None),
        P("segment", "expert", None, None),
    )
    out_specs = P("segment", "expert", None)
    return jax.shard_map(layer, mesh=mesh, in_specs=in_specs, out_specs=out_specs, check_vma=False)
```
